256 devices in a mesh: dp: 16 (over y_hi, z), ctx: 4 (over y_lo, core), uly: 4 (over x).
Axes of the slice: x: 4, y: 4 (y_hi: 2, y_lo: 2; y = y_hi * 2 + y_lo), z: 8, core: 2. Of those that a mesh axis runs over, the one named last changes fastest.
Arguments:
- queries: bfloat16 [16, 3072, 1536], P('dp', ('ctx', 'uly')), may hold values from -4.5 to 4.5
- key_rows: bfloat16 [16, 3072, 1536], P('dp', ('ctx', 'uly')), may hold values from -4.5 to 4.5
- value_rows: bfloat16 [16, 3072, 1536], P('dp', ('ctx', 'uly')), may hold values from -5 to 5
- out_grad: bfloat16 [16, 3072, 3072], P('dp', 'ctx'), may hold values from -6 to 6
- out_weight: bfloat16 [1536, 3072], P('uly'), may hold values from -0.15625 to 0.15625
- tile_lists: int32 [8, 6], replicated, may hold values from -1 to 7, as said below
- windows: int32 [12, 2], replicated, may hold values from 0 to 1, as said below
Outputs:
- query_grad: bfloat16 [16, 3072, 1536], P('dp', ('ctx', 'uly'))
- key_grad: bfloat16 [16, 3072, 1536], P('dp', ('ctx', 'uly'))
- value_grad: bfloat16 [16, 3072, 1536], P('dp', ('ctx', 'uly'))
- weight_grad: bfloat16 [1536, 3072], P('uly')
The draws below stay inside these ranges and needn't reach their ends.
Inputs may be any that keep to these rules, and one draw needn't show every extreme that they name: `tile_lists`: entry j of row Q = f * 2 + s is -1 or (f + j // 2 - 1) * 2 + j % 2; it is -1 wherever f + j // 2 - 1 lies outside 0 to 3, and never at an in-range entry with j % 2 == s. Of any two consecutive heads, at least one has windows[h, 0] = 1.
All inputs are finite; a program needn't handle non-finite values.
Results may differ from the reference program's by a relative error of at most 0.014.
Values may be sent and summed in bfloat16 or wider, within the bound.
No kernel may reach another device: no remote copies, remote signals or barrier semaphores. Data moves between devices by JAX's collectives and lax.ppermute only.
A program may use at most 192 MiB of HBM per device.

```python
import jax
import jax.numpy as jnp
from jax import lax

HEADS = 12
HD = 128
DOUT = 3072
TILE = 384
TW = 2
NFT = 4
QTILES = 8
CT = 3072
CLIPS = 16


def drawn_pair(key):
    base_key = jax.random.fold_in(key, 7)
    sub_keys = jax.random.split(base_key, 2)
    full_shape = (CLIPS, CT, HEADS * HD)
    query_out = jnp.clip(jax.random.normal(sub_keys[0], full_shape, jnp.float32), -4.5, 4.5)
    key_out = jnp.clip(jax.random.normal(sub_keys[1], full_shape, jnp.float32), -4.5, 4.5)
    return (query_out, key_out)


def draw_queries(key, part):
    return drawn_pair(key)[0].astype(jnp.bfloat16)


def draw_key_rows(key, part):
    return drawn_pair(key)[1].astype(jnp.bfloat16)


def draw_tile_lists(key, part):
    keep_key = jax.random.fold_in(key, 11)
    slot_ids = jnp.arange(3 * TW, dtype=jnp.int32)
    slot_time = slot_ids // TW - 1
    slot_space = slot_ids % TW
    tile_ids = jnp.arange(QTILES, dtype=jnp.int32)
    frame_of = tile_ids // TW
    spot_of = tile_ids % TW
    frame_to = frame_of[:, None] + slot_time[None, :]
    inside = (frame_to >= 0) & (frame_to < NFT)
    coin = jax.random.randint(keep_key, (QTILES, 3 * TW), 0, 2) == 1
    kept = coin | (slot_space[None, :] == spot_of[:, None])
    return jnp.where(inside & kept, frame_to * TW + slot_space[None, :], -1).astype(jnp.int32)


def draw_windows(key, part):
    sub_keys = jax.random.split(jax.random.fold_in(key, 23), 4)
    head_ids = jnp.arange(HEADS, dtype=jnp.int32)
    parity = jax.random.randint(sub_keys[0], (), 0, 2)
    time_bits = jax.random.randint(sub_keys[1], (HEADS,), 0, 2)
    first_free = 1 - parity
    temporal = jnp.where((head_ids + parity) % 2 == 0, 1, jnp.where(head_ids == first_free, 0, time_bits))
    zero_at = jax.random.randint(sub_keys[2], (), 0, HEADS)
    space_bits = jax.random.randint(sub_keys[3], (HEADS,), 0, 2)
    spatial = jnp.where(head_ids == zero_at, 0, jnp.where(head_ids == (zero_at + 1) % HEADS, 1, space_bits))
    return jnp.stack([temporal, spatial], axis=1).astype(jnp.int32)


def steps_of(rng, dims, cuts, least, top_value):
    gain, own = 1.0, jax.random.fold_in(rng, 6)
    for dim, blocks in cuts:
        steps = jnp.exp(jax.random.uniform(jax.random.fold_in(own, dim), (blocks,), jnp.float32, least / len(cuts), top_value / len(cuts)))
        gain = gain * jnp.repeat(steps, dims[dim] // blocks).reshape([-1 if axis == dim else 1 for axis in range(len(dims))])
    return gain


def centred(own_key, extent, deviation, most, cuts=(), kind=jnp.bfloat16):
    drawn = jax.random.normal(own_key, extent, jnp.float32) * deviation
    if len(cuts) > 0:
        drawn = steps_of(own_key, extent, cuts, -0.22, 0.18) * drawn
    return jnp.clip(drawn, min=-most, max=most).astype(kind)


def setup_inputs(seed: int = 0) -> dict:
    streams_of = jax.random.split(jax.random.key(seed), 8)
    queries = draw_queries(jax.random.fold_in(streams_of[7], 71), 0)
    key_rows = draw_key_rows(jax.random.fold_in(streams_of[7], 71), 0)
    value_rows = centred(streams_of[2], (CLIPS, CT, HEADS * HD), 1.0, 5.0, ((0, 16), (1, 16)))
    out_grad = centred(streams_of[3], (CLIPS, CT, DOUT), 1.0, 6.0, ((0, 16), (1, 4)))
    out_weight = centred(streams_of[4], (HEADS * HD, DOUT), (HEADS * HD) ** -0.5, 0.15625, ((0, 4),))
    tile_lists = draw_tile_lists(jax.random.fold_in(streams_of[7], 71), 0)
    windows = draw_windows(jax.random.fold_in(streams_of[7], 71), 0)
    return {"queries": queries, "key_rows": key_rows, "value_rows": value_rows, "out_grad": out_grad, "out_weight": out_weight, "tile_lists": tile_lists, "windows": windows}


def cross_rounded(parts):
    lowered = lax.optimization_barrier(parts.astype(jnp.bfloat16)).astype(jnp.float32)
    return jnp.concatenate([lowered[0:1], parts[1:2], lowered[2:3]], axis=0)


def softmax_block(query_tile, key_window, allow):
    scaling = HD ** -0.5
    score_grid = (jnp.dot(query_tile, key_window.T, preferred_element_type=jnp.float32) * scaling).reshape(TW, TILE, 3 * TW, TILE)
    key_mask = allow[:, None, :, None]
    row_max = jnp.max(jnp.where(key_mask, score_grid, -jnp.inf), axis=(2, 3), keepdims=True)
    raised = jnp.where(key_mask, jnp.exp(score_grid - row_max), 0.0)
    totals = jnp.sum(raised, axis=(2, 3), keepdims=True)
    return (raised / totals).reshape(TW * TILE, 3 * TW * TILE)


def block_pass(query_tile, key_window, value_window, grad_tile, allow):
    scaling = HD ** -0.5
    mixing = softmax_block(query_tile, key_window, allow)
    mixing_low = mixing.astype(jnp.bfloat16)
    out_low = jnp.dot(mixing_low, value_window, preferred_element_type=jnp.float32).astype(jnp.bfloat16)
    row_delta = jnp.sum(out_low.astype(jnp.float32) * grad_tile.astype(jnp.float32), axis=1, keepdims=True)
    value_part = jnp.dot(mixing_low.T, grad_tile, preferred_element_type=jnp.float32)
    prob_grad = jnp.dot(grad_tile, value_window.T, preferred_element_type=jnp.float32)
    score_grad = (mixing * (prob_grad - row_delta) * scaling).astype(jnp.bfloat16)
    query_part = jnp.dot(score_grad, key_window, preferred_element_type=jnp.float32)
    key_part = jnp.dot(score_grad.T, query_tile, preferred_element_type=jnp.float32)
    return out_low, query_part, key_part, value_part


def head_pass(query_head, key_head, value_head, grad_head, allow_head):
    layer_rows = TW * TILE
    zero_frame = jnp.zeros((1, layer_rows, HD), jnp.bfloat16)
    key_padded = jnp.concatenate([zero_frame, key_head, zero_frame], axis=0)
    value_padded = jnp.concatenate([zero_frame, value_head, zero_frame], axis=0)

    def frame_step(carried, frame_at):
        key_total, value_total = carried
        key_window = lax.dynamic_slice_in_dim(key_padded, frame_at, 3, 0).reshape(3 * layer_rows, HD)
        value_window = lax.dynamic_slice_in_dim(value_padded, frame_at, 3, 0).reshape(3 * layer_rows, HD)
        query_tile = lax.dynamic_index_in_dim(query_head, frame_at, 0, keepdims=False)
        grad_tile = lax.dynamic_index_in_dim(grad_head, frame_at, 0, keepdims=False)
        allow = lax.dynamic_index_in_dim(allow_head, frame_at, 0, keepdims=False)
        out_low, query_part, key_part, value_part = block_pass(query_tile, key_window, value_window, grad_tile, allow)
        key_terms = cross_rounded(key_part.reshape(3, layer_rows, HD))
        value_terms = cross_rounded(value_part.reshape(3, layer_rows, HD))
        key_total = lax.dynamic_update_slice_in_dim(key_total, lax.dynamic_slice_in_dim(key_total, frame_at, 3, 0) + key_terms, frame_at, 0)
        value_total = lax.dynamic_update_slice_in_dim(value_total, lax.dynamic_slice_in_dim(value_total, frame_at, 3, 0) + value_terms, frame_at, 0)
        return (key_total, value_total), (out_low, query_part.astype(jnp.bfloat16))

    start_totals = jnp.zeros((NFT + 2, layer_rows, HD), jnp.float32)
    finals, stacked = lax.scan(frame_step, (start_totals, start_totals), jnp.arange(NFT, dtype=jnp.int32))
    key_total, value_total = finals
    outputs, query_grads = stacked
    return outputs, query_grads, key_total[1:-1].astype(jnp.bfloat16), value_total[1:-1].astype(jnp.bfloat16)


def reference(queries, key_rows, value_rows, out_grad, out_weight, tile_lists, windows):
    layer_rows = TW * TILE
    slot_ids = jnp.arange(3 * TW, dtype=jnp.int32)
    slot_time = slot_ids // TW - 1
    slot_space = slot_ids % TW
    tile_ids = jnp.arange(QTILES, dtype=jnp.int32)
    frame_of = tile_ids // TW
    spot_of = tile_ids % TW
    target = (frame_of[:, None] + slot_time[None, :]) * TW + slot_space[None, :]
    listed = (tile_lists == target) & (tile_lists >= 0)
    near_time = jnp.abs(slot_time)[None, None, :] <= windows[:, 0][:, None, None]
    near_space = jnp.abs(slot_space[None, :] - spot_of[:, None])[None, :, :] <= windows[:, 1][:, None, None]
    allowed = (listed[None] & near_time & near_space).reshape(HEADS, NFT, TW, 3 * TW)

    def head_view(token_rows):
        return token_rows.reshape(NFT, layer_rows, HEADS, HD).transpose(2, 0, 1, 3)

    def token_view(per_head):
        return per_head.transpose(1, 2, 0, 3).reshape(CT, HEADS * HD)

    def head_call(head_items):
        return head_pass(*head_items)

    def clip_step(grand_total, clip_items):
        query_clip, key_clip, value_clip, grad_clip = clip_items
        grad_out = jnp.dot(grad_clip, out_weight.T, preferred_element_type=jnp.float32).astype(jnp.bfloat16)
        outputs, query_grads, key_grads, value_grads = lax.map(head_call, (head_view(query_clip), head_view(key_clip), head_view(value_clip), head_view(grad_out), allowed))
        attended = token_view(outputs)
        grand_total = grand_total + jnp.dot(attended.T, grad_clip, preferred_element_type=jnp.float32)
        return grand_total, (token_view(query_grads), token_view(key_grads), token_view(value_grads))

    start_total = jnp.zeros((HEADS * HD, DOUT), jnp.float32)
    grand_total, grads = lax.scan(clip_step, start_total, (queries, key_rows, value_rows, out_grad))
    query_grad, key_grad, value_grad = grads
    return query_grad, key_grad, value_grad, (grand_total / CLIPS).astype(jnp.bfloat16)
```

```python
import jax
import jax.numpy as jnp
from jax import lax
from jax.sharding import PartitionSpec as P

HEADS = 12
HD = 128
TILE = 384
TW = 2
FT_DEV = 1


def extended(x, sides, width):
    for axis, dim in sides:
        count, length = (lax.axis_size(axis), x.shape[dim])
        up = [(i, (i + 1) % count) for i in range(count - 1)]
        down = [(j, i) for i, j in up]
        last = lax.slice_in_dim(x, length - width, length, axis=dim)
        initial = lax.slice_in_dim(x, 0, width, axis=dim)
        before = lax.ppermute(last, axis, up)
        after = lax.ppermute(initial, axis, down)
        x = jnp.concatenate([before, x, after], axis=dim)
    return x


def cross_rounded(parts):
    lowered = lax.optimization_barrier(parts.astype(jnp.bfloat16)).astype(jnp.float32)
    return jnp.concatenate([lowered[0:1], parts[1:2], lowered[2:3]], axis=0)


def score_grid_of(query_tile, key_window):
    scaling = HD ** (-0.5)
    scores = jnp.dot(query_tile, key_window.T, preferred_element_type=jnp.float32) * scaling
    return scores.reshape(TW, TILE, 3 * TW, TILE)


def forward_block(query_tile, key_window, value_window, allow):
    score_grid = score_grid_of(query_tile, key_window)
    key_mask = allow[:, None, :, None]
    row_max = jnp.max(jnp.where(key_mask, score_grid, -jnp.inf), axis=(2, 3), keepdims=True)
    raised = jnp.where(key_mask, jnp.exp(score_grid - row_max), 0.0)
    totals = jnp.sum(raised, axis=(2, 3), keepdims=True)
    mixing = (raised / totals).reshape(TW * TILE, 3 * TW * TILE)
    out_low = jnp.dot(
        mixing.astype(jnp.bfloat16), value_window, preferred_element_type=jnp.float32
    ).astype(jnp.bfloat16)
    return (mixing, out_low, row_max, totals)


def backward_block(query_tile, key_window, value_window, grad_tile, mixing, out_low):
    scaling = HD ** (-0.5)
    mixing_low = mixing.astype(jnp.bfloat16)
    row_delta = jnp.sum(
        out_low.astype(jnp.float32) * grad_tile.astype(jnp.float32), axis=1, keepdims=True
    )
    value_part = lax.dot_general(
        mixing_low, grad_tile, (((0,), (0,)), ((), ())), preferred_element_type=jnp.float32
    )
    prob_grad = jnp.dot(grad_tile, value_window.T, preferred_element_type=jnp.float32)
    score_grad = (mixing * (prob_grad - row_delta) * scaling).astype(jnp.bfloat16)
    query_part = jnp.dot(score_grad, key_window, preferred_element_type=jnp.float32)
    key_part = lax.dot_general(
        score_grad, query_tile, (((0,), (0,)), ((), ())), preferred_element_type=jnp.float32
    )
    return (query_part, key_part, value_part)


def weight_sum(attended, token_grads):
    local_term = lax.dot_general(
        attended, token_grads, (((0,), (0,)), ((), ())), preferred_element_type=jnp.float32
    )
    rows, cols = local_term.shape
    part = lax.psum_scatter(local_term, ("dp", "ctx"), scatter_dimension=1, tiled=True)
    part = (part / lax.axis_size("dp")).astype(jnp.bfloat16)
    whole = lax.all_gather(part, ("dp", "ctx"), axis=1, tiled=True)
    return whole.reshape(rows, cols)


def on_device(queries, key_rows, value_rows, out_grad, out_weight, tile_lists, windows):
    heads_here = HEADS // lax.axis_size("uly")
    width_here = heads_here * HD
    layer_rows = TW * TILE
    span_rows = FT_DEV * layer_rows
    query_heads, pair_heads = (
        lax.all_to_all(queries[None], "uly", split_axis=3, concat_axis=2, tiled=True),
        lax.all_to_all(
            jnp.stack([key_rows, value_rows]), "uly", split_axis=3, concat_axis=2, tiled=True
        ),
    )
    query_heads = query_heads.reshape(FT_DEV, layer_rows, heads_here, HD)
    window = extended(pair_heads, (("ctx", 1),), 1)
    window = window.reshape(2, FT_DEV + 2, layer_rows, heads_here, HD)
    grad_out = lax.dot_general(
        out_grad[0], out_weight, (((1,), (1,)), ((), ())), preferred_element_type=jnp.float32
    )
    grad_out = grad_out.astype(jnp.bfloat16).reshape(FT_DEV, layer_rows, heads_here, HD)
    ctx_at = lax.axis_index("ctx")
    uly_at = lax.axis_index("uly")
    list_rows = lax.dynamic_slice_in_dim(tile_lists, ctx_at * (FT_DEV * TW), FT_DEV * TW, 0)
    listed = (list_rows >= 0).reshape(FT_DEV, TW, 3 * TW)
    reach_rows = lax.dynamic_slice_in_dim(windows, uly_at * heads_here, heads_here, 0)
    slot_ids = jnp.arange(3 * TW, dtype=jnp.int32)
    slot_time = slot_ids // TW - 1
    slot_space = slot_ids % TW
    spot_ids = jnp.arange(TW, dtype=jnp.int32)
    near_time = jnp.abs(slot_time)[None, :] <= reach_rows[:, 0:1]
    near_space = (
        jnp.abs(slot_space[None, :] - spot_ids[:, None])[None, :, :]
        <= reach_rows[:, 1][:, None, None]
    )
    allowed = listed[:, None, :, :] & near_time[None, :, None, :] & near_space[None, :, :, :]

    def tiles_of(frame_at, head_at):
        query_tile = query_heads[frame_at, :, head_at]
        key_window = window[0, frame_at : frame_at + 3, :, head_at].reshape(3 * layer_rows, HD)
        value_window = window[1, frame_at : frame_at + 3, :, head_at].reshape(3 * layer_rows, HD)
        return (query_tile, key_window, value_window)

    def assemble(per_block):
        frames_list = [jnp.stack(per_block[0], axis=1)]
        return jnp.stack(frames_list, axis=0).reshape(span_rows, width_here)

    pair_total = jnp.zeros((2, FT_DEV + 2, layer_rows, heads_here, HD), jnp.float32)
    out_blocks = [[None] * heads_here]
    query_blocks = [[None] * heads_here]

    def add_back(pair_total, frame_at, head_at, mixing, out_low):
        query_tile, key_window, value_window = tiles_of(frame_at, head_at)
        query_part, key_part, value_part = backward_block(
            query_tile, key_window, value_window, grad_out[frame_at, :, head_at], mixing, out_low
        )
        query_blocks[frame_at][head_at] = query_part.astype(jnp.bfloat16)
        pair_total = pair_total.at[0, frame_at : frame_at + 3, :, head_at].add(
            cross_rounded(key_part.reshape(3, layer_rows, HD))
        )
        pair_total = pair_total.at[1, frame_at : frame_at + 3, :, head_at].add(
            cross_rounded(value_part.reshape(3, layer_rows, HD))
        )
        return pair_total

    frame_at = 0
    saved = []
    for head_at in range(heads_here):
        query_tile, key_window, value_window = tiles_of(frame_at, head_at)
        mixing, out_low, row_max, totals = forward_block(
            query_tile, key_window, value_window, allowed[frame_at, head_at]
        )
        out_blocks[frame_at][head_at] = out_low
        saved.append((mixing, out_low))
    attended = assemble(out_blocks)
    weight_grad = weight_sum(attended, out_grad[0])
    for head_at in range(heads_here):
        mixing, out_low = saved[head_at]
        pair_total = add_back(pair_total, frame_at, head_at, mixing, out_low)
    outgoing = jnp.stack([pair_total[:, 0], pair_total[:, FT_DEV + 1]]).astype(jnp.bfloat16)
    returned = extended(outgoing, (("ctx", 0),), 1).astype(jnp.float32)
    own_grads = pair_total[:, 1 : FT_DEV + 1]
    own_grads = own_grads.at[:, 0].add(returned[0])
    own_grads = own_grads.at[:, FT_DEV - 1].add(returned[3])
    key_heads = own_grads[0].reshape(1, span_rows, width_here).astype(jnp.bfloat16)
    value_heads = own_grads[1].reshape(1, span_rows, width_here).astype(jnp.bfloat16)
    query_grad_heads = assemble(query_blocks).reshape(1, span_rows, width_here)
    tokens_back = (
        lax.all_to_all(query_grad_heads, "uly", split_axis=1, concat_axis=2, tiled=True),
        lax.all_to_all(key_heads, "uly", split_axis=1, concat_axis=2, tiled=True),
        lax.all_to_all(value_heads, "uly", split_axis=1, concat_axis=2, tiled=True),
    )
    return (tokens_back[0], tokens_back[1], tokens_back[2], weight_grad)


def solution(mesh):
    in_specs = (
        P("dp", ("ctx", "uly"), None),
        P("dp", ("ctx", "uly"), None),
        P("dp", ("ctx", "uly"), None),
        P("dp", "ctx", None),
        P("uly", None),
        P(),
        P(),
    )
    out_specs = (
        P("dp", ("ctx", "uly"), None),
        P("dp", ("ctx", "uly"), None),
        P("dp", ("ctx", "uly"), None),
        P("uly", None),
    )
    return jax.shard_map(
        on_device, mesh=mesh, in_specs=in_specs, out_specs=out_specs, check_vma=False
    )
```

```python
import jax
import jax.numpy as jnp
from jax import lax
from jax.sharding import PartitionSpec as P

HEADS = 12
HD = 128
TILE = 384
TW = 2
FT_DEV = 1


def extended(x, sides, width):
    for axis, dim in sides:
        count, length = (lax.axis_size(axis), x.shape[dim])
        up = [(i, (i + 1) % count) for i in range(count - 1)]
        down = [(j, i) for i, j in up]
        last = lax.slice_in_dim(x, length - width, length, axis=dim)
        initial = lax.slice_in_dim(x, 0, width, axis=dim)
        before = lax.ppermute(last, axis, up)
        after = lax.ppermute(initial, axis, down)
        x = jnp.concatenate([before, x, after], axis=dim)
    return x


def cross_rounded(parts):
    lowered = lax.optimization_barrier(parts.astype(jnp.bfloat16)).astype(jnp.float32)
    return jnp.concatenate([lowered[0:1], parts[1:2], lowered[2:3]], axis=0)


def score_grid_of(query_tile, key_window):
    scaling = HD ** (-0.5)
    scores = jnp.dot(query_tile, key_window.T, preferred_element_type=jnp.float32) * scaling
    return scores.reshape(TW, TILE, 3 * TW, TILE)


def forward_block(query_tile, key_window, value_window, allow):
    score_grid = score_grid_of(query_tile, key_window)
    key_mask = allow[:, None, :, None]
    row_max = jnp.max(jnp.where(key_mask, score_grid, -jnp.inf), axis=(2, 3), keepdims=True)
    raised = jnp.where(key_mask, jnp.exp(score_grid - row_max), 0.0)
    totals = jnp.sum(raised, axis=(2, 3), keepdims=True)
    mixing = (raised / totals).reshape(TW * TILE, 3 * TW * TILE)
    out_low = jnp.dot(
        mixing.astype(jnp.bfloat16), value_window, preferred_element_type=jnp.float32
    ).astype(jnp.bfloat16)
    return (mixing, out_low, row_max, totals)


def backward_block(query_tile, key_window, value_window, grad_tile, mixing, out_low):
    scaling = HD ** (-0.5)
    mixing_low = mixing.astype(jnp.bfloat16)
    row_delta = jnp.sum(
        out_low.astype(jnp.float32) * grad_tile.astype(jnp.float32), axis=1, keepdims=True
    )
    value_part = lax.dot_general(
        mixing_low, grad_tile, (((0,), (0,)), ((), ())), preferred_element_type=jnp.float32
    )
    prob_grad = jnp.dot(grad_tile, value_window.T, preferred_element_type=jnp.float32)
    score_grad = (mixing * (prob_grad - row_delta) * scaling).astype(jnp.bfloat16)
    query_part = jnp.dot(score_grad, key_window, preferred_element_type=jnp.float32)
    key_part = lax.dot_general(
        score_grad, query_tile, (((0,), (0,)), ((), ())), preferred_element_type=jnp.float32
    )
    return (query_part, key_part, value_part)


def weight_sum(local_term):
    grand_total = lax.psum(local_term, ("dp", "ctx"))
    return (grand_total / lax.axis_size("dp")).astype(jnp.bfloat16)


def on_device(queries, key_rows, value_rows, out_grad, out_weight, tile_lists, windows):
    heads_here = HEADS // lax.axis_size("uly")
    width_here = heads_here * HD
    layer_rows = TW * TILE
    span_rows = FT_DEV * layer_rows
    query_heads, pair_heads = (
        lax.all_to_all(queries[None], "uly", split_axis=3, concat_axis=2, tiled=True),
        lax.all_to_all(
            jnp.stack([key_rows, value_rows]), "uly", split_axis=3, concat_axis=2, tiled=True
        ),
    )
    query_heads = query_heads.reshape(FT_DEV, layer_rows, heads_here, HD)
    window = extended(pair_heads, (("ctx", 1),), 1)
    window = window.reshape(2, FT_DEV + 2, layer_rows, heads_here, HD)
    grad_out = lax.dot_general(
        out_grad[0], out_weight, (((1,), (1,)), ((), ())), preferred_element_type=jnp.float32
    )
    grad_out = grad_out.astype(jnp.bfloat16).reshape(FT_DEV, layer_rows, heads_here, HD)
    ctx_at = lax.axis_index("ctx")
    uly_at = lax.axis_index("uly")
    list_rows = lax.dynamic_slice_in_dim(tile_lists, ctx_at * (FT_DEV * TW), FT_DEV * TW, 0)
    listed = (list_rows >= 0).reshape(FT_DEV, TW, 3 * TW)
    reach_rows = lax.dynamic_slice_in_dim(windows, uly_at * heads_here, heads_here, 0)
    slot_ids = jnp.arange(3 * TW, dtype=jnp.int32)
    slot_time = slot_ids // TW - 1
    slot_space = slot_ids % TW
    spot_ids = jnp.arange(TW, dtype=jnp.int32)
    near_time = jnp.abs(slot_time)[None, :] <= reach_rows[:, 0:1]
    near_space = (
        jnp.abs(slot_space[None, :] - spot_ids[:, None])[None, :, :]
        <= reach_rows[:, 1][:, None, None]
    )
    allowed = listed[:, None, :, :] & near_time[None, :, None, :] & near_space[None, :, :, :]

    def tiles_of(frame_at, head_at):
        query_tile = query_heads[frame_at, :, head_at]
        key_window = window[0, frame_at : frame_at + 3, :, head_at].reshape(3 * layer_rows, HD)
        value_window = window[1, frame_at : frame_at + 3, :, head_at].reshape(3 * layer_rows, HD)
        return (query_tile, key_window, value_window)

    def assemble(per_block):
        frames_list = [jnp.stack(per_block[0], axis=1)]
        return jnp.stack(frames_list, axis=0).reshape(span_rows, width_here)

    pair_total = jnp.zeros((2, FT_DEV + 2, layer_rows, heads_here, HD), jnp.float32)
    out_blocks = [[None] * heads_here]
    query_blocks = [[None] * heads_here]

    def add_back(pair_total, frame_at, head_at, mixing, out_low):
        query_tile, key_window, value_window = tiles_of(frame_at, head_at)
        query_part, key_part, value_part = backward_block(
            query_tile, key_window, value_window, grad_out[frame_at, :, head_at], mixing, out_low
        )
        query_blocks[frame_at][head_at] = query_part.astype(jnp.bfloat16)
        pair_total = pair_total.at[0, frame_at : frame_at + 3, :, head_at].add(
            cross_rounded(key_part.reshape(3, layer_rows, HD))
        )
        pair_total = pair_total.at[1, frame_at : frame_at + 3, :, head_at].add(
            cross_rounded(value_part.reshape(3, layer_rows, HD))
        )
        return pair_total

    frame_at = 0
    saved = []
    weight_parts = []
    for head_at in range(heads_here):
        query_tile, key_window, value_window = tiles_of(frame_at, head_at)
        mixing, out_low, row_max, totals = forward_block(
            query_tile, key_window, value_window, allowed[frame_at, head_at]
        )
        out_blocks[frame_at][head_at] = out_low
        saved.append((mixing, out_low))
    attended = assemble(out_blocks)
    local_term = lax.dot_general(
        attended, out_grad[0], (((0,), (0,)), ((), ())), preferred_element_type=jnp.float32
    )
    local_term, saved = lax.optimization_barrier((local_term, saved))
    weight_grad = weight_sum(local_term)
    for head_at in range(heads_here):
        mixing, out_low = saved[head_at]
        pair_total = add_back(pair_total, frame_at, head_at, mixing, out_low)
    outgoing = jnp.stack([pair_total[:, 0], pair_total[:, FT_DEV + 1]]).astype(jnp.bfloat16)
    returned = extended(outgoing, (("ctx", 0),), 1).astype(jnp.float32)
    own_grads = pair_total[:, 1 : FT_DEV + 1]
    own_grads = own_grads.at[:, 0].add(returned[0])
    own_grads = own_grads.at[:, FT_DEV - 1].add(returned[3])
    key_heads = own_grads[0].reshape(1, span_rows, width_here).astype(jnp.bfloat16)
    value_heads = own_grads[1].reshape(1, span_rows, width_here).astype(jnp.bfloat16)
    query_grad_heads = assemble(query_blocks).reshape(1, span_rows, width_here)
    tokens_back = (
        lax.all_to_all(query_grad_heads, "uly", split_axis=1, concat_axis=2, tiled=True),
        lax.all_to_all(key_heads, "uly", split_axis=1, concat_axis=2, tiled=True),
        lax.all_to_all(value_heads, "uly", split_axis=1, concat_axis=2, tiled=True),
    )
    return (tokens_back[0], tokens_back[1], tokens_back[2], weight_grad)


def solution(mesh):
    in_specs = (
        P("dp", ("ctx", "uly"), None),
        P("dp", ("ctx", "uly"), None),
        P("dp", ("ctx", "uly"), None),
        P("dp", "ctx", None),
        P("uly", None),
        P(),
        P(),
    )
    out_specs = (
        P("dp", ("ctx", "uly"), None),
        P("dp", ("ctx", "uly"), None),
        P("dp", ("ctx", "uly"), None),
        P("uly", None),
    )
    return jax.shard_map(
        on_device, mesh=mesh, in_specs=in_specs, out_specs=out_specs, check_vma=False
    )
```

```python
import jax
import jax.numpy as jnp
from jax import lax
from jax.sharding import PartitionSpec as P

HEADS = 12
HD = 128
TILE = 384
TW = 2
FT_DEV = 1


def extended(x, sides, width):
    for axis, dim in sides:
        count, length = (lax.axis_size(axis), x.shape[dim])
        up = [(i, (i + 1) % count) for i in range(count - 1)]
        down = [(j, i) for i, j in up]
        last = lax.slice_in_dim(x, length - width, length, axis=dim)
        initial = lax.slice_in_dim(x, 0, width, axis=dim)
        before = lax.ppermute(last, axis, up)
        after = lax.ppermute(initial, axis, down)
        x = jnp.concatenate([before, x, after], axis=dim)
    return x


def cross_rounded(parts):
    lowered = lax.optimization_barrier(parts.astype(jnp.bfloat16)).astype(jnp.float32)
    return jnp.concatenate([lowered[0:1], parts[1:2], lowered[2:3]], axis=0)


def score_grid_of(query_tile, key_window):
    scaling = HD ** (-0.5)
    scores = jnp.dot(query_tile, key_window.T, preferred_element_type=jnp.float32) * scaling
    return scores.reshape(TW, TILE, 3 * TW, TILE)


def forward_block(query_tile, key_window, value_window, allow):
    score_grid = score_grid_of(query_tile, key_window)
    key_bias = jnp.where(allow, 0.0, -jnp.inf).astype(jnp.float32)[:, None, :, None]
    score_grid = score_grid + key_bias
    row_max = jnp.max(score_grid, axis=(2, 3), keepdims=True)
    raised = jnp.exp(score_grid - row_max)
    totals = jnp.sum(raised, axis=(2, 3), keepdims=True)
    mixing = (raised / totals).reshape(TW * TILE, 3 * TW * TILE)
    out_low = jnp.dot(
        mixing.astype(jnp.bfloat16), value_window, preferred_element_type=jnp.float32
    ).astype(jnp.bfloat16)
    return (mixing, out_low, row_max, totals)


def backward_block(query_tile, key_window, value_window, grad_tile, mixing, out_low):
    scaling = HD ** (-0.5)
    mixing_low = mixing.astype(jnp.bfloat16)
    row_delta = jnp.sum(
        out_low.astype(jnp.float32) * grad_tile.astype(jnp.float32), axis=1, keepdims=True
    )
    value_part = lax.dot_general(
        mixing_low, grad_tile, (((0,), (0,)), ((), ())), preferred_element_type=jnp.float32
    )
    prob_grad = jnp.dot(grad_tile, value_window.T, preferred_element_type=jnp.float32)
    score_grad = (mixing * (prob_grad - row_delta) * scaling).astype(jnp.bfloat16)
    query_part = jnp.dot(score_grad, key_window, preferred_element_type=jnp.float32)
    key_part = lax.dot_general(
        score_grad, query_tile, (((0,), (0,)), ((), ())), preferred_element_type=jnp.float32
    )
    return (query_part, key_part, value_part)


def weight_sum(local_term):
    grand_total = lax.psum(local_term, ("dp", "ctx"))
    return (grand_total / lax.axis_size("dp")).astype(jnp.bfloat16)


def to_heads(rows):
    count = lax.axis_size("uly")
    tokens, width = rows.shape[1], rows.shape[2]
    parts = rows[0].reshape(tokens, count, width // count).transpose(1, 0, 2)
    parts = lax.all_to_all(parts, "uly", 0, 0, tiled=True)
    return parts.reshape(count * tokens, width // count)


def to_tokens(per_head):
    count = lax.axis_size("uly")
    tokens, width = per_head.shape
    parts = per_head.reshape(count, tokens // count, width)
    parts = lax.all_to_all(parts, "uly", 0, 0, tiled=True)
    return parts.transpose(1, 0, 2).reshape(1, tokens // count, count * width)


def on_device(queries, key_rows, value_rows, out_grad, out_weight, tile_lists, windows):
    heads_here = HEADS // lax.axis_size("uly")
    layer_rows = TW * TILE
    query_heads = to_heads(queries)
    pair_heads = jnp.stack([to_heads(key_rows), to_heads(value_rows)])[:, None]
    window = extended(pair_heads, (("ctx", 1),), 1)
    grad_out = lax.dot_general(
        out_grad[0], out_weight, (((1,), (1,)), ((), ())), preferred_element_type=jnp.float32
    ).astype(jnp.bfloat16)
    ctx_at = lax.axis_index("ctx")
    uly_at = lax.axis_index("uly")
    list_rows = lax.dynamic_slice_in_dim(tile_lists, ctx_at * (FT_DEV * TW), FT_DEV * TW, 0)
    listed = (list_rows >= 0).reshape(FT_DEV, TW, 3 * TW)
    reach_rows = lax.dynamic_slice_in_dim(windows, uly_at * heads_here, heads_here, 0)
    slot_ids = jnp.arange(3 * TW, dtype=jnp.int32)
    slot_time = slot_ids // TW - 1
    slot_space = slot_ids % TW
    spot_ids = jnp.arange(TW, dtype=jnp.int32)
    near_time = jnp.abs(slot_time)[None, :] <= reach_rows[:, 0:1]
    near_space = (
        jnp.abs(slot_space[None, :] - spot_ids[:, None])[None, :, :]
        <= reach_rows[:, 1][:, None, None]
    )
    allowed = listed[:, None, :, :] & near_time[None, :, None, :] & near_space[None, :, :, :]

    def tiles_of(head_at):
        cols = slice(head_at * HD, (head_at + 1) * HD)
        query_tile = query_heads[:, cols]
        key_window = window[0, :, :, cols].reshape(3 * layer_rows, HD)
        value_window = window[1, :, :, cols].reshape(3 * layer_rows, HD)
        return (query_tile, key_window, value_window)

    saved = []
    out_blocks = []
    for head_at in range(heads_here):
        query_tile, key_window, value_window = tiles_of(head_at)
        mixing, out_low, row_max, totals = forward_block(
            query_tile, key_window, value_window, allowed[0, head_at]
        )
        out_blocks.append(out_low)
        saved.append((mixing, out_low))
    attended = jnp.concatenate(out_blocks, axis=1)
    local_term = lax.dot_general(
        attended, out_grad[0], (((0,), (0,)), ((), ())), preferred_element_type=jnp.float32
    )
    local_term, saved = lax.optimization_barrier((local_term, saved))
    weight_grad = weight_sum(local_term)
    query_blocks = []
    key_terms = []
    value_terms = []
    for head_at in range(heads_here):
        mixing, out_low = saved[head_at]
        query_tile, key_window, value_window = tiles_of(head_at)
        cols = slice(head_at * HD, (head_at + 1) * HD)
        query_part, key_part, value_part = backward_block(
            query_tile, key_window, value_window, grad_out[:, cols], mixing, out_low
        )
        query_blocks.append(query_part.astype(jnp.bfloat16))
        key_terms.append(cross_rounded(key_part.reshape(3, layer_rows, HD)))
        value_terms.append(cross_rounded(value_part.reshape(3, layer_rows, HD)))
    pair_total = jnp.stack(
        [jnp.concatenate(key_terms, axis=2), jnp.concatenate(value_terms, axis=2)]
    )
    outgoing = jnp.stack([pair_total[:, 0], pair_total[:, 2]]).astype(jnp.bfloat16)
    returned = extended(outgoing, (("ctx", 0),), 1).astype(jnp.float32)
    own_grads = pair_total[:, 1] + returned[0]
    own_grads = own_grads + returned[3]
    key_heads = own_grads[0].astype(jnp.bfloat16)
    value_heads = own_grads[1].astype(jnp.bfloat16)
    query_grad_heads = jnp.concatenate(query_blocks, axis=1)
    return (
        to_tokens(query_grad_heads),
        to_tokens(key_heads),
        to_tokens(value_heads),
        weight_grad,
    )


def solution(mesh):
    in_specs = (
        P("dp", ("ctx", "uly"), None),
        P("dp", ("ctx", "uly"), None),
        P("dp", ("ctx", "uly"), None),
        P("dp", "ctx", None),
        P("uly", None),
        P(),
        P(),
    )
    out_specs = (
        P("dp", ("ctx", "uly"), None),
        P("dp", ("ctx", "uly"), None),
        P("dp", ("ctx", "uly"), None),
        P("uly", None),
    )
    return jax.shard_map(
        on_device, mesh=mesh, in_specs=in_specs, out_specs=out_specs, check_vma=False
    )
```

```python
import jax
import jax.numpy as jnp
from jax import lax
from jax.sharding import PartitionSpec as P

HEADS = 12
HD = 128
TILE = 384
TW = 2
FT_DEV = 1


def extended(x, sides, width):
    for axis, dim in sides:
        count, length = (lax.axis_size(axis), x.shape[dim])
        up = [(i, (i + 1) % count) for i in range(count - 1)]
        down = [(j, i) for i, j in up]
        last = lax.slice_in_dim(x, length - width, length, axis=dim)
        initial = lax.slice_in_dim(x, 0, width, axis=dim)
        before = lax.ppermute(last, axis, up)
        after = lax.ppermute(initial, axis, down)
        x = jnp.concatenate([before, x, after], axis=dim)
    return x


def cross_rounded(parts):
    lowered = lax.optimization_barrier(parts.astype(jnp.bfloat16)).astype(jnp.float32)
    return jnp.concatenate([lowered[0:1], parts[1:2], lowered[2:3]], axis=0)


def forward_block(query_tile, key_window, value_window, allow):
    scaling = HD ** (-0.5)
    scores = jnp.dot(query_tile, key_window.T, preferred_element_type=jnp.float32) * scaling
    col_bias = jnp.repeat(jnp.where(allow, 0.0, -jnp.inf).astype(jnp.float32), TILE, axis=1)
    row_spot = lax.broadcasted_iota(jnp.int32, (TW * TILE, 1), 0) // TILE
    key_bias = col_bias[0][None, :]
    for spot in range(1, TW):
        key_bias = jnp.where(row_spot == spot, col_bias[spot][None, :], key_bias)
    scores = scores + key_bias
    row_max = jnp.max(scores, axis=1, keepdims=True)
    raised = jnp.exp(scores - row_max)
    totals = jnp.sum(raised, axis=1, keepdims=True)
    mixing = raised / totals
    out_low = jnp.dot(
        mixing.astype(jnp.bfloat16), value_window, preferred_element_type=jnp.float32
    ).astype(jnp.bfloat16)
    return (mixing, out_low, row_max, totals)


def backward_block(query_tile, key_window, value_window, grad_tile, mixing, out_low):
    scaling = HD ** (-0.5)
    mixing_low = mixing.astype(jnp.bfloat16)
    row_delta = jnp.sum(
        out_low.astype(jnp.float32) * grad_tile.astype(jnp.float32), axis=1, keepdims=True
    )
    value_part = lax.dot_general(
        mixing_low, grad_tile, (((0,), (0,)), ((), ())), preferred_element_type=jnp.float32
    )
    prob_grad = jnp.dot(grad_tile, value_window.T, preferred_element_type=jnp.float32)
    score_grad = (mixing * (prob_grad - row_delta) * scaling).astype(jnp.bfloat16)
    query_part = jnp.dot(score_grad, key_window, preferred_element_type=jnp.float32)
    key_part = lax.dot_general(
        score_grad, query_tile, (((0,), (0,)), ((), ())), preferred_element_type=jnp.float32
    )
    return (query_part, key_part, value_part)


def weight_sum(local_term):
    grand_total = lax.psum(local_term, ("dp", "ctx"))
    return (grand_total / lax.axis_size("dp")).astype(jnp.bfloat16)


def to_heads(rows):
    count = lax.axis_size("uly")
    tokens, width = rows.shape[1], rows.shape[2]
    parts = rows[0].reshape(tokens, count, width // count).transpose(1, 0, 2)
    parts = lax.all_to_all(parts, "uly", 0, 0, tiled=True)
    return parts.reshape(count * tokens, width // count)


def to_tokens(per_head):
    count = lax.axis_size("uly")
    tokens, width = per_head.shape
    parts = per_head.reshape(count, tokens // count, width)
    parts = lax.all_to_all(parts, "uly", 0, 0, tiled=True)
    return parts.transpose(1, 0, 2).reshape(1, tokens // count, count * width)


def on_device(queries, key_rows, value_rows, out_grad, out_weight, tile_lists, windows):
    heads_here = HEADS // lax.axis_size("uly")
    layer_rows = TW * TILE
    query_heads = to_heads(queries)
    pair_heads = jnp.stack([to_heads(key_rows), to_heads(value_rows)])[:, None]
    window = extended(pair_heads, (("ctx", 1),), 1)
    ctx_at = lax.axis_index("ctx")
    uly_at = lax.axis_index("uly")
    list_rows = lax.dynamic_slice_in_dim(tile_lists, ctx_at * (FT_DEV * TW), FT_DEV * TW, 0)
    listed = (list_rows >= 0).reshape(FT_DEV, TW, 3 * TW)
    reach_rows = lax.dynamic_slice_in_dim(windows, uly_at * heads_here, heads_here, 0)
    slot_ids = jnp.arange(3 * TW, dtype=jnp.int32)
    slot_time = slot_ids // TW - 1
    slot_space = slot_ids % TW
    spot_ids = jnp.arange(TW, dtype=jnp.int32)
    near_time = jnp.abs(slot_time)[None, :] <= reach_rows[:, 0:1]
    near_space = (
        jnp.abs(slot_space[None, :] - spot_ids[:, None])[None, :, :]
        <= reach_rows[:, 1][:, None, None]
    )
    allowed = listed[:, None, :, :] & near_time[None, :, None, :] & near_space[None, :, :, :]

    def tiles_of(head_at):
        cols = slice(head_at * HD, (head_at + 1) * HD)
        query_tile = query_heads[:, cols]
        key_window = window[0, :, :, cols].reshape(3 * layer_rows, HD)
        value_window = window[1, :, :, cols].reshape(3 * layer_rows, HD)
        return (query_tile, key_window, value_window)

    saved = []
    out_blocks = []
    for head_at in range(heads_here):
        query_tile, key_window, value_window = tiles_of(head_at)
        mixing, out_low, row_max, totals = forward_block(
            query_tile, key_window, value_window, allowed[0, head_at]
        )
        out_blocks.append(out_low)
        saved.append((mixing, out_low))
    attended = jnp.concatenate(out_blocks, axis=1)
    local_term = lax.dot_general(
        attended, out_grad[0], (((0,), (0,)), ((), ())), preferred_element_type=jnp.float32
    )
    local_term, saved, token_grads = lax.optimization_barrier((local_term, saved, out_grad[0]))
    weight_grad = weight_sum(local_term)
    grad_out = lax.dot_general(
        token_grads, out_weight, (((1,), (1,)), ((), ())), preferred_element_type=jnp.float32
    ).astype(jnp.bfloat16)
    query_blocks = []
    key_terms = []
    value_terms = []
    for head_at in range(heads_here):
        mixing, out_low = saved[head_at]
        query_tile, key_window, value_window = tiles_of(head_at)
        cols = slice(head_at * HD, (head_at + 1) * HD)
        query_part, key_part, value_part = backward_block(
            query_tile, key_window, value_window, grad_out[:, cols], mixing, out_low
        )
        query_blocks.append(query_part.astype(jnp.bfloat16))
        key_terms.append(cross_rounded(key_part.reshape(3, layer_rows, HD)))
        value_terms.append(cross_rounded(value_part.reshape(3, layer_rows, HD)))
    pair_total = jnp.stack(
        [jnp.concatenate(key_terms, axis=2), jnp.concatenate(value_terms, axis=2)]
    )
    outgoing = jnp.stack([pair_total[:, 0], pair_total[:, 2]]).astype(jnp.bfloat16)
    returned = extended(outgoing, (("ctx", 0),), 1).astype(jnp.float32)
    own_grads = pair_total[:, 1] + returned[0]
    own_grads = own_grads + returned[3]
    key_heads = own_grads[0].astype(jnp.bfloat16)
    value_heads = own_grads[1].astype(jnp.bfloat16)
    query_grad_heads = jnp.concatenate(query_blocks, axis=1)
    return (
        to_tokens(query_grad_heads),
        to_tokens(key_heads),
        to_tokens(value_heads),
        weight_grad,
    )


def solution(mesh):
    in_specs = (
        P("dp", ("ctx", "uly"), None),
        P("dp", ("ctx", "uly"), None),
        P("dp", ("ctx", "uly"), None),
        P("dp", "ctx", None),
        P("uly", None),
        P(),
        P(),
    )
    out_specs = (
        P("dp", ("ctx", "uly"), None),
        P("dp", ("ctx", "uly"), None),
        P("dp", ("ctx", "uly"), None),
        P("uly", None),
    )
    return jax.shard_map(
        on_device, mesh=mesh, in_specs=in_specs, out_specs=out_specs, check_vma=False
    )
```

```python
import jax
import jax.numpy as jnp
from jax import lax
from jax.sharding import PartitionSpec as P

HEADS = 12
HD = 128
TILE = 384
TW = 2
FT_DEV = 1


def extended(x, sides, width):
    for axis, dim in sides:
        count, length = (lax.axis_size(axis), x.shape[dim])
        up = [(i, (i + 1) % count) for i in range(count - 1)]
        down = [(j, i) for i, j in up]
        last = lax.slice_in_dim(x, length - width, length, axis=dim)
        initial = lax.slice_in_dim(x, 0, width, axis=dim)
        before = lax.ppermute(last, axis, up)
        after = lax.ppermute(initial, axis, down)
        x = jnp.concatenate([before, x, after], axis=dim)
    return x


def cross_rounded(parts):
    lowered = lax.optimization_barrier(parts.astype(jnp.bfloat16)).astype(jnp.float32)
    return jnp.concatenate([lowered[0:1], parts[1:2], lowered[2:3]], axis=0)


def forward_block(query_tile, key_window, value_window, allow):
    scaling = HD ** (-0.5)
    scores = jnp.dot(query_tile, key_window.T, preferred_element_type=jnp.float32) * scaling
    col_bias = jnp.repeat(jnp.where(allow, 0.0, -jnp.inf).astype(jnp.float32), TILE, axis=1)
    row_spot = lax.broadcasted_iota(jnp.int32, (TW * TILE, 1), 0) // TILE
    key_bias = col_bias[0][None, :]
    for spot in range(1, TW):
        key_bias = jnp.where(row_spot == spot, col_bias[spot][None, :], key_bias)
    scores = scores + key_bias
    row_max = jnp.max(scores, axis=1, keepdims=True)
    raised = jnp.exp(scores - row_max)
    totals = jnp.sum(raised, axis=1, keepdims=True)
    mixing = raised / totals
    out_low = jnp.dot(
        mixing.astype(jnp.bfloat16), value_window, preferred_element_type=jnp.float32
    ).astype(jnp.bfloat16)
    return (mixing, out_low, row_max, totals)


def backward_block(query_tile, key_window, value_window, grad_tile, mixing, out_low):
    scaling = HD ** (-0.5)
    mixing_low = mixing.astype(jnp.bfloat16)
    row_delta = jnp.sum(
        out_low.astype(jnp.float32) * grad_tile.astype(jnp.float32), axis=1, keepdims=True
    )
    value_part = lax.dot_general(
        mixing_low, grad_tile, (((0,), (0,)), ((), ())), preferred_element_type=jnp.float32
    )
    prob_grad = jnp.dot(grad_tile, value_window.T, preferred_element_type=jnp.float32)
    score_grad = (mixing * (prob_grad - row_delta) * scaling).astype(jnp.bfloat16)
    query_part = jnp.dot(score_grad, key_window, preferred_element_type=jnp.float32)
    key_part = lax.dot_general(
        score_grad, query_tile, (((0,), (0,)), ((), ())), preferred_element_type=jnp.float32
    )
    return (query_part, key_part, value_part)


def gathered_sum(local_term):
    groups = ("dp", "ctx")
    rows, cols = local_term.shape
    count = lax.axis_size("dp") * lax.axis_size("ctx")
    row_blocks = 8
    col_blocks = count // row_blocks
    blocks = local_term.reshape(row_blocks, rows // row_blocks, col_blocks, cols // col_blocks)
    blocks = blocks.transpose(0, 2, 1, 3).reshape(count, rows // row_blocks, cols // col_blocks)
    blocks = lax.all_to_all(blocks.astype(jnp.bfloat16), groups, 0, 0, tiled=True)
    owned = jnp.sum(blocks.astype(jnp.float32), axis=0) / lax.axis_size("dp")
    owned = owned.astype(jnp.bfloat16)
    spread = jnp.broadcast_to(owned[None], (count,) + owned.shape)
    gathered = lax.all_to_all(spread, groups, 0, 0, tiled=True)
    gathered = gathered.reshape(row_blocks, col_blocks, rows // row_blocks, cols // col_blocks)
    return gathered.transpose(0, 2, 1, 3).reshape(rows, cols)


def weight_sum(local_term):
    split = local_term.shape[0] - HD
    grand_total = lax.psum(local_term[:split], ("dp", "ctx"))
    reduced = (grand_total / lax.axis_size("dp")).astype(jnp.bfloat16)
    return jnp.concatenate([reduced, gathered_sum(local_term[split:])], axis=0)


def to_heads(rows):
    count = lax.axis_size("uly")
    tokens, width = rows.shape[1], rows.shape[2]
    parts = rows[0].reshape(tokens, count, width // count).transpose(1, 0, 2)
    parts = lax.all_to_all(parts, "uly", 0, 0, tiled=True)
    return parts.reshape(count * tokens, width // count)


def to_tokens(per_head):
    count = lax.axis_size("uly")
    tokens, width = per_head.shape
    parts = per_head.reshape(count, tokens // count, width)
    parts = lax.all_to_all(parts, "uly", 0, 0, tiled=True)
    return parts.transpose(1, 0, 2).reshape(1, tokens // count, count * width)


def on_device(queries, key_rows, value_rows, out_grad, out_weight, tile_lists, windows):
    heads_here = HEADS // lax.axis_size("uly")
    layer_rows = TW * TILE
    query_heads = to_heads(queries)
    pair_heads = jnp.stack([to_heads(key_rows), to_heads(value_rows)])[:, None]
    window = extended(pair_heads, (("ctx", 1),), 1)
    ctx_at = lax.axis_index("ctx")
    uly_at = lax.axis_index("uly")
    list_rows = lax.dynamic_slice_in_dim(tile_lists, ctx_at * (FT_DEV * TW), FT_DEV * TW, 0)
    listed = (list_rows >= 0).reshape(FT_DEV, TW, 3 * TW)
    reach_rows = lax.dynamic_slice_in_dim(windows, uly_at * heads_here, heads_here, 0)
    slot_ids = jnp.arange(3 * TW, dtype=jnp.int32)
    slot_time = slot_ids // TW - 1
    slot_space = slot_ids % TW
    spot_ids = jnp.arange(TW, dtype=jnp.int32)
    near_time = jnp.abs(slot_time)[None, :] <= reach_rows[:, 0:1]
    near_space = (
        jnp.abs(slot_space[None, :] - spot_ids[:, None])[None, :, :]
        <= reach_rows[:, 1][:, None, None]
    )
    allowed = listed[:, None, :, :] & near_time[None, :, None, :] & near_space[None, :, :, :]

    def tiles_of(head_at):
        cols = slice(head_at * HD, (head_at + 1) * HD)
        query_tile = query_heads[:, cols]
        key_window = window[0, :, :, cols].reshape(3 * layer_rows, HD)
        value_window = window[1, :, :, cols].reshape(3 * layer_rows, HD)
        return (query_tile, key_window, value_window)

    saved = []
    out_blocks = []
    for head_at in range(heads_here):
        query_tile, key_window, value_window = tiles_of(head_at)
        mixing, out_low, row_max, totals = forward_block(
            query_tile, key_window, value_window, allowed[0, head_at]
        )
        out_blocks.append(out_low)
        saved.append((mixing, out_low))
    attended = jnp.concatenate(out_blocks, axis=1)
    local_term = lax.dot_general(
        attended, out_grad[0], (((0,), (0,)), ((), ())), preferred_element_type=jnp.float32
    )
    local_term, saved, token_grads = lax.optimization_barrier((local_term, saved, out_grad[0]))
    weight_grad = weight_sum(local_term)
    grad_out = lax.dot_general(
        token_grads, out_weight, (((1,), (1,)), ((), ())), preferred_element_type=jnp.float32
    ).astype(jnp.bfloat16)
    query_blocks = []
    key_terms = []
    value_terms = []
    for head_at in range(heads_here):
        mixing, out_low = saved[head_at]
        query_tile, key_window, value_window = tiles_of(head_at)
        cols = slice(head_at * HD, (head_at + 1) * HD)
        query_part, key_part, value_part = backward_block(
            query_tile, key_window, value_window, grad_out[:, cols], mixing, out_low
        )
        query_blocks.append(query_part.astype(jnp.bfloat16))
        key_terms.append(cross_rounded(key_part.reshape(3, layer_rows, HD)))
        value_terms.append(cross_rounded(value_part.reshape(3, layer_rows, HD)))
    pair_total = jnp.stack(
        [jnp.concatenate(key_terms, axis=2), jnp.concatenate(value_terms, axis=2)]
    )
    outgoing = jnp.stack([pair_total[:, 0], pair_total[:, 2]]).astype(jnp.bfloat16)
    returned = extended(outgoing, (("ctx", 0),), 1).astype(jnp.float32)
    own_grads = pair_total[:, 1] + returned[0]
    own_grads = own_grads + returned[3]
    key_heads = own_grads[0].astype(jnp.bfloat16)
    value_heads = own_grads[1].astype(jnp.bfloat16)
    query_grad_heads = jnp.concatenate(query_blocks, axis=1)
    return (
        to_tokens(query_grad_heads),
        to_tokens(key_heads),
        to_tokens(value_heads),
        weight_grad,
    )


def solution(mesh):
    in_specs = (
        P("dp", ("ctx", "uly"), None),
        P("dp", ("ctx", "uly"), None),
        P("dp", ("ctx", "uly"), None),
        P("dp", "ctx", None),
        P("uly", None),
        P(),
        P(),
    )
    out_specs = (
        P("dp", ("ctx", "uly"), None),
        P("dp", ("ctx", "uly"), None),
        P("dp", ("ctx", "uly"), None),
        P("uly", None),
    )
    return jax.shard_map(
        on_device, mesh=mesh, in_specs=in_specs, out_specs=out_specs, check_vma=False
    )
```

```python
import jax
import jax.numpy as jnp
from jax import lax
from jax.sharding import PartitionSpec as P

HEADS = 12
HD = 128
TILE = 384
TW = 2
FT_DEV = 1


def extended(x, sides, width):
    for axis, dim in sides:
        count, length = (lax.axis_size(axis), x.shape[dim])
        up = [(i, (i + 1) % count) for i in range(count - 1)]
        down = [(j, i) for i, j in up]
        last = lax.slice_in_dim(x, length - width, length, axis=dim)
        initial = lax.slice_in_dim(x, 0, width, axis=dim)
        before = lax.ppermute(last, axis, up)
        after = lax.ppermute(initial, axis, down)
        x = jnp.concatenate([before, x, after], axis=dim)
    return x


def cross_rounded(parts):
    lowered = lax.optimization_barrier(parts.astype(jnp.bfloat16)).astype(jnp.float32)
    return jnp.concatenate([lowered[0:1], parts[1:2], lowered[2:3]], axis=0)


def forward_block(query_tile, key_window, value_window, allow):
    scaling = HD ** (-0.5)
    scores = jnp.dot(query_tile, key_window.T, preferred_element_type=jnp.float32) * scaling
    col_bias = jnp.repeat(jnp.where(allow, 0.0, -jnp.inf).astype(jnp.float32), TILE, axis=1)
    row_spot = lax.broadcasted_iota(jnp.int32, (TW * TILE, 1), 0) // TILE
    key_bias = col_bias[0][None, :]
    for spot in range(1, TW):
        key_bias = jnp.where(row_spot == spot, col_bias[spot][None, :], key_bias)
    scores = scores + key_bias
    row_max = jnp.max(scores, axis=1, keepdims=True)
    raised = jnp.exp(scores - row_max)
    totals = jnp.sum(raised, axis=1, keepdims=True)
    mixing = raised / totals
    out_low = jnp.dot(
        mixing.astype(jnp.bfloat16), value_window, preferred_element_type=jnp.float32
    ).astype(jnp.bfloat16)
    return (mixing, out_low, row_max, totals)


def backward_block(query_tile, key_window, value_window, grad_tile, mixing, out_low):
    scaling = HD ** (-0.5)
    mixing_low = mixing.astype(jnp.bfloat16)
    row_delta = jnp.sum(
        out_low.astype(jnp.float32) * grad_tile.astype(jnp.float32), axis=1, keepdims=True
    )
    value_part = lax.dot_general(
        mixing_low, grad_tile, (((0,), (0,)), ((), ())), preferred_element_type=jnp.float32
    )
    prob_grad = jnp.dot(grad_tile, value_window.T, preferred_element_type=jnp.float32)
    score_grad = (mixing * (prob_grad - row_delta) * scaling).astype(jnp.bfloat16)
    query_part = jnp.dot(score_grad, key_window, preferred_element_type=jnp.float32)
    key_part = lax.dot_general(
        score_grad, query_tile, (((0,), (0,)), ((), ())), preferred_element_type=jnp.float32
    )
    return (query_part, key_part, value_part)


def weight_sum(local_term):
    grand_total = lax.psum(lax.psum(local_term, "ctx"), "dp")
    return (grand_total / lax.axis_size("dp")).astype(jnp.bfloat16)


def to_heads(rows):
    count = lax.axis_size("uly")
    tokens, width = rows.shape[1], rows.shape[2]
    parts = rows[0].reshape(tokens, count, width // count).transpose(1, 0, 2)
    parts = lax.all_to_all(parts, "uly", 0, 0, tiled=True)
    return parts.reshape(count * tokens, width // count)


def to_tokens(per_head):
    count = lax.axis_size("uly")
    tokens, width = per_head.shape
    parts = per_head.reshape(count, tokens // count, width)
    parts = lax.all_to_all(parts, "uly", 0, 0, tiled=True)
    return parts.transpose(1, 0, 2).reshape(1, tokens // count, count * width)


def on_device(queries, key_rows, value_rows, out_grad, out_weight, tile_lists, windows):
    heads_here = HEADS // lax.axis_size("uly")
    layer_rows = TW * TILE
    query_heads = to_heads(queries)
    pair_heads = jnp.stack([to_heads(key_rows), to_heads(value_rows)])[:, None]
    window = extended(pair_heads, (("ctx", 1),), 1)
    ctx_at = lax.axis_index("ctx")
    uly_at = lax.axis_index("uly")
    list_rows = lax.dynamic_slice_in_dim(tile_lists, ctx_at * (FT_DEV * TW), FT_DEV * TW, 0)
    listed = (list_rows >= 0).reshape(FT_DEV, TW, 3 * TW)
    reach_rows = lax.dynamic_slice_in_dim(windows, uly_at * heads_here, heads_here, 0)
    slot_ids = jnp.arange(3 * TW, dtype=jnp.int32)
    slot_time = slot_ids // TW - 1
    slot_space = slot_ids % TW
    spot_ids = jnp.arange(TW, dtype=jnp.int32)
    near_time = jnp.abs(slot_time)[None, :] <= reach_rows[:, 0:1]
    near_space = (
        jnp.abs(slot_space[None, :] - spot_ids[:, None])[None, :, :]
        <= reach_rows[:, 1][:, None, None]
    )
    allowed = listed[:, None, :, :] & near_time[None, :, None, :] & near_space[None, :, :, :]

    def tiles_of(head_at):
        cols = slice(head_at * HD, (head_at + 1) * HD)
        query_tile = query_heads[:, cols]
        key_window = window[0, :, :, cols].reshape(3 * layer_rows, HD)
        value_window = window[1, :, :, cols].reshape(3 * layer_rows, HD)
        return (query_tile, key_window, value_window)

    saved = []
    out_blocks = []
    for head_at in range(heads_here):
        query_tile, key_window, value_window = tiles_of(head_at)
        mixing, out_low, row_max, totals = forward_block(
            query_tile, key_window, value_window, allowed[0, head_at]
        )
        out_blocks.append(out_low)
        saved.append((mixing, out_low))
    attended = jnp.concatenate(out_blocks, axis=1)
    local_term = lax.dot_general(
        attended, out_grad[0], (((0,), (0,)), ((), ())), preferred_element_type=jnp.float32
    )
    local_term, saved, token_grads = lax.optimization_barrier((local_term, saved, out_grad[0]))
    weight_grad = weight_sum(local_term)
    grad_out = lax.dot_general(
        token_grads, out_weight, (((1,), (1,)), ((), ())), preferred_element_type=jnp.float32
    ).astype(jnp.bfloat16)
    query_blocks = []
    key_terms = []
    value_terms = []
    for head_at in range(heads_here):
        mixing, out_low = saved[head_at]
        query_tile, key_window, value_window = tiles_of(head_at)
        cols = slice(head_at * HD, (head_at + 1) * HD)
        query_part, key_part, value_part = backward_block(
            query_tile, key_window, value_window, grad_out[:, cols], mixing, out_low
        )
        query_blocks.append(query_part.astype(jnp.bfloat16))
        key_terms.append(cross_rounded(key_part.reshape(3, layer_rows, HD)))
        value_terms.append(cross_rounded(value_part.reshape(3, layer_rows, HD)))
    pair_total = jnp.stack(
        [jnp.concatenate(key_terms, axis=2), jnp.concatenate(value_terms, axis=2)]
    )
    outgoing = jnp.stack([pair_total[:, 0], pair_total[:, 2]]).astype(jnp.bfloat16)
    returned = extended(outgoing, (("ctx", 0),), 1).astype(jnp.float32)
    own_grads = pair_total[:, 1] + returned[0]
    own_grads = own_grads + returned[3]
    key_heads = own_grads[0].astype(jnp.bfloat16)
    value_heads = own_grads[1].astype(jnp.bfloat16)
    query_grad_heads = jnp.concatenate(query_blocks, axis=1)
    return (
        to_tokens(query_grad_heads),
        to_tokens(key_heads),
        to_tokens(value_heads),
        weight_grad,
    )


def solution(mesh):
    in_specs = (
        P("dp", ("ctx", "uly"), None),
        P("dp", ("ctx", "uly"), None),
        P("dp", ("ctx", "uly"), None),
        P("dp", "ctx", None),
        P("uly", None),
        P(),
        P(),
    )
    out_specs = (
        P("dp", ("ctx", "uly"), None),
        P("dp", ("ctx", "uly"), None),
        P("dp", ("ctx", "uly"), None),
        P("uly", None),
    )
    return jax.shard_map(
        on_device, mesh=mesh, in_specs=in_specs, out_specs=out_specs, check_vma=False
    )
```

```python
import jax
import jax.numpy as jnp
from jax import lax
from jax.sharding import PartitionSpec as P

HEADS = 12
HD = 128
TILE = 384
TW = 2
FT_DEV = 1


def extended(x, sides, width):
    for axis, dim in sides:
        count, length = (lax.axis_size(axis), x.shape[dim])
        up = [(i, (i + 1) % count) for i in range(count - 1)]
        down = [(j, i) for i, j in up]
        last = lax.slice_in_dim(x, length - width, length, axis=dim)
        initial = lax.slice_in_dim(x, 0, width, axis=dim)
        before = lax.ppermute(last, axis, up)
        after = lax.ppermute(initial, axis, down)
        x = jnp.concatenate([before, x, after], axis=dim)
    return x


def cross_rounded(parts):
    lowered = lax.optimization_barrier(parts.astype(jnp.bfloat16)).astype(jnp.float32)
    return jnp.concatenate([lowered[0:1], parts[1:2], lowered[2:3]], axis=0)


def forward_block(query_tile, key_window, value_window, allow):
    scaling = HD ** (-0.5)
    scores = jnp.dot(query_tile, key_window.T, preferred_element_type=jnp.float32) * scaling
    col_bias = jnp.repeat(jnp.where(allow, 0.0, -jnp.inf).astype(jnp.float32), TILE, axis=1)
    row_spot = lax.broadcasted_iota(jnp.int32, (TW * TILE, 1), 0) // TILE
    key_bias = col_bias[0][None, :]
    for spot in range(1, TW):
        key_bias = jnp.where(row_spot == spot, col_bias[spot][None, :], key_bias)
    scores = scores + key_bias
    row_max = jnp.max(scores, axis=1, keepdims=True)
    raised = jnp.exp(scores - row_max)
    totals = jnp.sum(raised, axis=1, keepdims=True)
    mixing = raised / totals
    out_low = jnp.dot(
        mixing.astype(jnp.bfloat16), value_window, preferred_element_type=jnp.float32
    ).astype(jnp.bfloat16)
    return (mixing, out_low, row_max, totals)


def backward_block(query_tile, key_window, value_window, grad_tile, mixing, out_low):
    scaling = HD ** (-0.5)
    mixing_low = mixing.astype(jnp.bfloat16)
    row_delta = jnp.sum(
        out_low.astype(jnp.float32) * grad_tile.astype(jnp.float32), axis=1, keepdims=True
    )
    value_part = lax.dot_general(
        mixing_low, grad_tile, (((0,), (0,)), ((), ())), preferred_element_type=jnp.float32
    )
    prob_grad = jnp.dot(grad_tile, value_window.T, preferred_element_type=jnp.float32)
    score_grad = (mixing * (prob_grad - row_delta) * scaling).astype(jnp.bfloat16)
    query_part = jnp.dot(score_grad, key_window, preferred_element_type=jnp.float32)
    key_part = lax.dot_general(
        score_grad, query_tile, (((0,), (0,)), ((), ())), preferred_element_type=jnp.float32
    )
    return (query_part, key_part, value_part)


def weight_sum(local_term):
    grand_total = lax.psum(local_term, ("dp", "ctx"))
    return (grand_total / lax.axis_size("dp")).astype(jnp.bfloat16)


def to_heads(*arrays):
    count = lax.axis_size("uly")
    tokens, width = arrays[0].shape[1], arrays[0].shape[2]
    parts = jnp.stack(
        [rows[0].reshape(tokens, count, width // count).transpose(1, 0, 2) for rows in arrays],
        axis=1,
    )
    parts = lax.all_to_all(parts, "uly", 0, 0, tiled=True)
    return [parts[:, at].reshape(count * tokens, width // count) for at in range(len(arrays))]


def to_tokens(per_head):
    count = lax.axis_size("uly")
    tokens, width = per_head.shape
    parts = per_head.reshape(count, tokens // count, width)
    parts = lax.all_to_all(parts, "uly", 0, 0, tiled=True)
    return parts.transpose(1, 0, 2).reshape(1, tokens // count, count * width)


def on_device(queries, key_rows, value_rows, out_grad, out_weight, tile_lists, windows):
    heads_here = HEADS // lax.axis_size("uly")
    layer_rows = TW * TILE
    query_heads, key_heads, value_heads = to_heads(queries, key_rows, value_rows)
    pair_heads = jnp.stack([key_heads, value_heads])[:, None]
    window = extended(pair_heads, (("ctx", 1),), 1)
    ctx_at = lax.axis_index("ctx")
    uly_at = lax.axis_index("uly")
    list_rows = lax.dynamic_slice_in_dim(tile_lists, ctx_at * (FT_DEV * TW), FT_DEV * TW, 0)
    listed = (list_rows >= 0).reshape(FT_DEV, TW, 3 * TW)
    reach_rows = lax.dynamic_slice_in_dim(windows, uly_at * heads_here, heads_here, 0)
    slot_ids = jnp.arange(3 * TW, dtype=jnp.int32)
    slot_time = slot_ids // TW - 1
    slot_space = slot_ids % TW
    spot_ids = jnp.arange(TW, dtype=jnp.int32)
    near_time = jnp.abs(slot_time)[None, :] <= reach_rows[:, 0:1]
    near_space = (
        jnp.abs(slot_space[None, :] - spot_ids[:, None])[None, :, :]
        <= reach_rows[:, 1][:, None, None]
    )
    allowed = listed[:, None, :, :] & near_time[None, :, None, :] & near_space[None, :, :, :]

    def tiles_of(head_at):
        cols = slice(head_at * HD, (head_at + 1) * HD)
        query_tile = query_heads[:, cols]
        key_window = window[0, :, :, cols].reshape(3 * layer_rows, HD)
        value_window = window[1, :, :, cols].reshape(3 * layer_rows, HD)
        return (query_tile, key_window, value_window)

    saved = []
    out_blocks = []
    for head_at in range(heads_here):
        query_tile, key_window, value_window = tiles_of(head_at)
        mixing, out_low, row_max, totals = forward_block(
            query_tile, key_window, value_window, allowed[0, head_at]
        )
        out_blocks.append(out_low)
        saved.append((mixing, out_low))
    attended = jnp.concatenate(out_blocks, axis=1)
    local_term = lax.dot_general(
        attended, out_grad[0], (((0,), (0,)), ((), ())), preferred_element_type=jnp.float32
    )
    local_term, saved, token_grads = lax.optimization_barrier((local_term, saved, out_grad[0]))
    weight_grad = weight_sum(local_term)
    grad_out = lax.dot_general(
        token_grads, out_weight, (((1,), (1,)), ((), ())), preferred_element_type=jnp.float32
    ).astype(jnp.bfloat16)
    query_blocks = []
    key_terms = []
    value_terms = []
    for head_at in range(heads_here):
        mixing, out_low = saved[head_at]
        query_tile, key_window, value_window = tiles_of(head_at)
        cols = slice(head_at * HD, (head_at + 1) * HD)
        query_part, key_part, value_part = backward_block(
            query_tile, key_window, value_window, grad_out[:, cols], mixing, out_low
        )
        query_blocks.append(query_part.astype(jnp.bfloat16))
        key_terms.append(cross_rounded(key_part.reshape(3, layer_rows, HD)))
        value_terms.append(cross_rounded(value_part.reshape(3, layer_rows, HD)))
    pair_total = jnp.stack(
        [jnp.concatenate(key_terms, axis=2), jnp.concatenate(value_terms, axis=2)]
    )
    outgoing = jnp.stack([pair_total[:, 0], pair_total[:, 2]]).astype(jnp.bfloat16)
    returned = extended(outgoing, (("ctx", 0),), 1).astype(jnp.float32)
    own_grads = pair_total[:, 1] + returned[0]
    own_grads = own_grads + returned[3]
    key_heads = own_grads[0].astype(jnp.bfloat16)
    value_heads = own_grads[1].astype(jnp.bfloat16)
    query_grad_heads = jnp.concatenate(query_blocks, axis=1)
    return (
        to_tokens(query_grad_heads),
        to_tokens(key_heads),
        to_tokens(value_heads),
        weight_grad,
    )


def solution(mesh):
    in_specs = (
        P("dp", ("ctx", "uly"), None),
        P("dp", ("ctx", "uly"), None),
        P("dp", ("ctx", "uly"), None),
        P("dp", "ctx", None),
        P("uly", None),
        P(),
        P(),
    )
    out_specs = (
        P("dp", ("ctx", "uly"), None),
        P("dp", ("ctx", "uly"), None),
        P("dp", ("ctx", "uly"), None),
        P("uly", None),
    )
    return jax.shard_map(
        on_device, mesh=mesh, in_specs=in_specs, out_specs=out_specs, check_vma=False
    )
```

```python
import jax
import jax.numpy as jnp
from jax import lax
from jax.sharding import PartitionSpec as P

HEADS = 12
HD = 128
TILE = 384
TW = 2
FT_DEV = 1


def extended(x, sides, width):
    for axis, dim in sides:
        count, length = (lax.axis_size(axis), x.shape[dim])
        up = [(i, (i + 1) % count) for i in range(count - 1)]
        down = [(j, i) for i, j in up]
        last = lax.slice_in_dim(x, length - width, length, axis=dim)
        initial = lax.slice_in_dim(x, 0, width, axis=dim)
        before = lax.ppermute(last, axis, up)
        after = lax.ppermute(initial, axis, down)
        x = jnp.concatenate([before, x, after], axis=dim)
    return x


def cross_rounded(parts):
    lowered = lax.optimization_barrier(parts.astype(jnp.bfloat16)).astype(jnp.float32)
    return jnp.concatenate([lowered[0:1], parts[1:2], lowered[2:3]], axis=0)


def forward_block(query_tile, key_window, value_window, allow):
    scaling = HD ** (-0.5)
    scores = jnp.dot(query_tile, key_window.T, preferred_element_type=jnp.float32) * scaling
    col_bias = jnp.repeat(jnp.where(allow, 0.0, -jnp.inf).astype(jnp.float32), TILE, axis=1)
    row_spot = lax.broadcasted_iota(jnp.int32, (TW * TILE, 1), 0) // TILE
    key_bias = col_bias[0][None, :]
    for spot in range(1, TW):
        key_bias = jnp.where(row_spot == spot, col_bias[spot][None, :], key_bias)
    scores = scores + key_bias
    row_max = jnp.max(scores, axis=1, keepdims=True)
    raised = jnp.exp(scores - row_max)
    totals = jnp.sum(raised, axis=1, keepdims=True)
    mixing = raised / totals
    out_low = jnp.dot(
        mixing.astype(jnp.bfloat16), value_window, preferred_element_type=jnp.float32
    ).astype(jnp.bfloat16)
    return (mixing, out_low, row_max, totals)


def backward_block(query_tile, key_window, value_window, grad_tile, mixing, out_low):
    scaling = HD ** (-0.5)
    mixing_low = mixing.astype(jnp.bfloat16)
    row_delta = jnp.sum(
        out_low.astype(jnp.float32) * grad_tile.astype(jnp.float32), axis=1, keepdims=True
    )
    value_part = lax.dot_general(
        mixing_low, grad_tile, (((0,), (0,)), ((), ())), preferred_element_type=jnp.float32
    )
    prob_grad = jnp.dot(grad_tile, value_window.T, preferred_element_type=jnp.float32)
    score_grad = (mixing * (prob_grad - row_delta) * scaling).astype(jnp.bfloat16)
    query_part = jnp.dot(score_grad, key_window, preferred_element_type=jnp.float32)
    key_part = lax.dot_general(
        score_grad, query_tile, (((0,), (0,)), ((), ())), preferred_element_type=jnp.float32
    )
    return (query_part, key_part, value_part)


def weight_sum(local_term):
    grand_total = lax.psum(local_term, ("dp", "ctx"))
    return (grand_total / lax.axis_size("dp")).astype(jnp.bfloat16)


def to_heads(*arrays):
    count = lax.axis_size("uly")
    tokens, width = arrays[0].shape[1], arrays[0].shape[2]
    parts = jnp.stack(
        [rows[0].reshape(tokens, count, width // count).transpose(1, 0, 2) for rows in arrays],
        axis=1,
    )
    parts = lax.all_to_all(parts, "uly", 0, 0, tiled=True)
    return [parts[:, at].reshape(count * tokens, width // count) for at in range(len(arrays))]


def to_tokens(per_head):
    count = lax.axis_size("uly")
    tokens, width = per_head.shape
    parts = per_head.reshape(count, tokens // count, width)
    parts = lax.all_to_all(parts, "uly", 0, 0, tiled=True)
    return parts.transpose(1, 0, 2).reshape(1, tokens // count, count * width)


def on_device(queries, key_rows, value_rows, out_grad, out_weight, tile_lists, windows):
    heads_here = HEADS // lax.axis_size("uly")
    layer_rows = TW * TILE
    query_heads, key_heads, value_heads = to_heads(queries, key_rows, value_rows)
    near = extended(jnp.stack([key_rows, value_rows]), (("ctx", 1),), 1)
    key_prev, key_next, value_prev, value_next = to_heads(
        near[0, 0:1], near[0, 2:3], near[1, 0:1], near[1, 2:3]
    )
    window = jnp.stack(
        [
            jnp.stack([key_prev, key_heads, key_next]),
            jnp.stack([value_prev, value_heads, value_next]),
        ]
    )
    ctx_at = lax.axis_index("ctx")
    uly_at = lax.axis_index("uly")
    list_rows = lax.dynamic_slice_in_dim(tile_lists, ctx_at * (FT_DEV * TW), FT_DEV * TW, 0)
    listed = (list_rows >= 0).reshape(FT_DEV, TW, 3 * TW)
    reach_rows = lax.dynamic_slice_in_dim(windows, uly_at * heads_here, heads_here, 0)
    slot_ids = jnp.arange(3 * TW, dtype=jnp.int32)
    slot_time = slot_ids // TW - 1
    slot_space = slot_ids % TW
    spot_ids = jnp.arange(TW, dtype=jnp.int32)
    near_time = jnp.abs(slot_time)[None, :] <= reach_rows[:, 0:1]
    near_space = (
        jnp.abs(slot_space[None, :] - spot_ids[:, None])[None, :, :]
        <= reach_rows[:, 1][:, None, None]
    )
    allowed = listed[:, None, :, :] & near_time[None, :, None, :] & near_space[None, :, :, :]

    def tiles_of(head_at):
        cols = slice(head_at * HD, (head_at + 1) * HD)
        query_tile = query_heads[:, cols]
        key_window = window[0, :, :, cols].reshape(3 * layer_rows, HD)
        value_window = window[1, :, :, cols].reshape(3 * layer_rows, HD)
        return (query_tile, key_window, value_window)

    saved = []
    out_blocks = []
    for head_at in range(heads_here):
        query_tile, key_window, value_window = tiles_of(head_at)
        mixing, out_low, row_max, totals = forward_block(
            query_tile, key_window, value_window, allowed[0, head_at]
        )
        out_blocks.append(out_low)
        saved.append((mixing, out_low))
    attended = jnp.concatenate(out_blocks, axis=1)
    local_term = lax.dot_general(
        attended, out_grad[0], (((0,), (0,)), ((), ())), preferred_element_type=jnp.float32
    )
    local_term, saved, token_grads = lax.optimization_barrier((local_term, saved, out_grad[0]))
    weight_grad = weight_sum(local_term)
    grad_out = lax.dot_general(
        token_grads, out_weight, (((1,), (1,)), ((), ())), preferred_element_type=jnp.float32
    ).astype(jnp.bfloat16)
    query_blocks = []
    key_terms = []
    value_terms = []
    for head_at in range(heads_here):
        mixing, out_low = saved[head_at]
        query_tile, key_window, value_window = tiles_of(head_at)
        cols = slice(head_at * HD, (head_at + 1) * HD)
        query_part, key_part, value_part = backward_block(
            query_tile, key_window, value_window, grad_out[:, cols], mixing, out_low
        )
        query_blocks.append(query_part.astype(jnp.bfloat16))
        key_terms.append(cross_rounded(key_part.reshape(3, layer_rows, HD)))
        value_terms.append(cross_rounded(value_part.reshape(3, layer_rows, HD)))
    pair_total = jnp.stack(
        [jnp.concatenate(key_terms, axis=2), jnp.concatenate(value_terms, axis=2)]
    )
    outgoing = jnp.stack([pair_total[:, 0], pair_total[:, 2]]).astype(jnp.bfloat16)
    returned = extended(outgoing, (("ctx", 0),), 1).astype(jnp.float32)
    own_grads = pair_total[:, 1] + returned[0]
    own_grads = own_grads + returned[3]
    key_heads = own_grads[0].astype(jnp.bfloat16)
    value_heads = own_grads[1].astype(jnp.bfloat16)
    query_grad_heads = jnp.concatenate(query_blocks, axis=1)
    return (
        to_tokens(query_grad_heads),
        to_tokens(key_heads),
        to_tokens(value_heads),
        weight_grad,
    )


def solution(mesh):
    in_specs = (
        P("dp", ("ctx", "uly"), None),
        P("dp", ("ctx", "uly"), None),
        P("dp", ("ctx", "uly"), None),
        P("dp", "ctx", None),
        P("uly", None),
        P(),
        P(),
    )
    out_specs = (
        P("dp", ("ctx", "uly"), None),
        P("dp", ("ctx", "uly"), None),
        P("dp", ("ctx", "uly"), None),
        P("uly", None),
    )
    return jax.shard_map(
        on_device, mesh=mesh, in_specs=in_specs, out_specs=out_specs, check_vma=False
    )
```

```python
import jax
import jax.numpy as jnp
from jax import lax
from jax.sharding import PartitionSpec as P

HEADS = 12
HD = 128
TILE = 384
TW = 2
FT_DEV = 1


def extended(x, sides, width):
    for axis, dim in sides:
        count, length = (lax.axis_size(axis), x.shape[dim])
        up = [(i, (i + 1) % count) for i in range(count - 1)]
        down = [(j, i) for i, j in up]
        last = lax.slice_in_dim(x, length - width, length, axis=dim)
        initial = lax.slice_in_dim(x, 0, width, axis=dim)
        before = lax.ppermute(last, axis, up)
        after = lax.ppermute(initial, axis, down)
        x = jnp.concatenate([before, x, after], axis=dim)
    return x


def cross_rounded(parts):
    lowered = lax.optimization_barrier(parts.astype(jnp.bfloat16)).astype(jnp.float32)
    return jnp.concatenate([lowered[0:1], parts[1:2], lowered[2:3]], axis=0)


def forward_block(query_tile, key_window, value_window, allow):
    scaling = HD ** (-0.5)
    scores = jnp.dot(query_tile, key_window.T, preferred_element_type=jnp.float32) * scaling
    col_bias = jnp.repeat(jnp.where(allow, 0.0, -jnp.inf).astype(jnp.float32), TILE, axis=1)
    row_spot = lax.broadcasted_iota(jnp.int32, (TW * TILE, 1), 0) // TILE
    key_bias = col_bias[0][None, :]
    for spot in range(1, TW):
        key_bias = jnp.where(row_spot == spot, col_bias[spot][None, :], key_bias)
    scores = scores + key_bias
    row_max = jnp.max(scores, axis=1, keepdims=True)
    raised = jnp.exp(scores - row_max)
    totals = jnp.sum(raised, axis=1, keepdims=True)
    mixing = raised / totals
    out_low = jnp.dot(
        mixing.astype(jnp.bfloat16), value_window, preferred_element_type=jnp.float32
    ).astype(jnp.bfloat16)
    return (mixing, out_low, row_max, totals)


def backward_block(query_tile, key_window, value_window, grad_tile, mixing, out_low):
    scaling = HD ** (-0.5)
    mixing_low = mixing.astype(jnp.bfloat16)
    row_delta = jnp.sum(
        out_low.astype(jnp.float32) * grad_tile.astype(jnp.float32), axis=1, keepdims=True
    )
    value_part = lax.dot_general(
        mixing_low, grad_tile, (((0,), (0,)), ((), ())), preferred_element_type=jnp.float32
    )
    prob_grad = jnp.dot(grad_tile, value_window.T, preferred_element_type=jnp.float32)
    score_grad = (mixing * (prob_grad - row_delta) * scaling).astype(jnp.bfloat16)
    query_part = jnp.dot(score_grad, key_window, preferred_element_type=jnp.float32)
    key_part = lax.dot_general(
        score_grad, query_tile, (((0,), (0,)), ((), ())), preferred_element_type=jnp.float32
    )
    return (query_part, key_part, value_part)


def weight_sum(local_term):
    grand_total = lax.psum(local_term, ("dp", "ctx"))
    return (grand_total / lax.axis_size("dp")).astype(jnp.bfloat16)


def to_heads(*arrays):
    count = lax.axis_size("uly")
    tokens, width = arrays[0].shape[1], arrays[0].shape[2]
    part = width // count
    parts = jnp.concatenate(
        [rows[0].reshape(tokens, count, part).transpose(1, 0, 2) for rows in arrays], axis=2
    )
    parts = lax.all_to_all(parts, "uly", 0, 0, tiled=True)
    return [
        parts[:, :, at * part : (at + 1) * part].reshape(count * tokens, part)
        for at in range(len(arrays))
    ]


def to_tokens(per_head):
    count = lax.axis_size("uly")
    tokens, width = per_head.shape
    parts = per_head.reshape(count, tokens // count, width)
    parts = lax.all_to_all(parts, "uly", 0, 0, tiled=True)
    return parts.transpose(1, 0, 2).reshape(1, tokens // count, count * width)


def on_device(queries, key_rows, value_rows, out_grad, out_weight, tile_lists, windows):
    heads_here = HEADS // lax.axis_size("uly")
    layer_rows = TW * TILE
    query_heads, key_heads, value_heads = to_heads(queries, key_rows, value_rows)
    pair_heads = jnp.stack([key_heads, value_heads])[:, None]
    window = extended(pair_heads, (("ctx", 1),), 1)
    ctx_at = lax.axis_index("ctx")
    uly_at = lax.axis_index("uly")
    list_rows = lax.dynamic_slice_in_dim(tile_lists, ctx_at * (FT_DEV * TW), FT_DEV * TW, 0)
    listed = (list_rows >= 0).reshape(FT_DEV, TW, 3 * TW)
    reach_rows = lax.dynamic_slice_in_dim(windows, uly_at * heads_here, heads_here, 0)
    slot_ids = jnp.arange(3 * TW, dtype=jnp.int32)
    slot_time = slot_ids // TW - 1
    slot_space = slot_ids % TW
    spot_ids = jnp.arange(TW, dtype=jnp.int32)
    near_time = jnp.abs(slot_time)[None, :] <= reach_rows[:, 0:1]
    near_space = (
        jnp.abs(slot_space[None, :] - spot_ids[:, None])[None, :, :]
        <= reach_rows[:, 1][:, None, None]
    )
    allowed = listed[:, None, :, :] & near_time[None, :, None, :] & near_space[None, :, :, :]

    def tiles_of(head_at):
        cols = slice(head_at * HD, (head_at + 1) * HD)
        query_tile = query_heads[:, cols]
        key_window = window[0, :, :, cols].reshape(3 * layer_rows, HD)
        value_window = window[1, :, :, cols].reshape(3 * layer_rows, HD)
        return (query_tile, key_window, value_window)

    saved = []
    out_blocks = []
    for head_at in range(heads_here):
        query_tile, key_window, value_window = tiles_of(head_at)
        mixing, out_low, row_max, totals = forward_block(
            query_tile, key_window, value_window, allowed[0, head_at]
        )
        out_blocks.append(out_low)
        saved.append((mixing, out_low))
    attended = jnp.concatenate(out_blocks, axis=1)
    local_term = lax.dot_general(
        attended, out_grad[0], (((0,), (0,)), ((), ())), preferred_element_type=jnp.float32
    )
    local_term, saved, token_grads = lax.optimization_barrier((local_term, saved, out_grad[0]))
    weight_grad = weight_sum(local_term)
    grad_out = lax.dot_general(
        token_grads, out_weight, (((1,), (1,)), ((), ())), preferred_element_type=jnp.float32
    ).astype(jnp.bfloat16)
    query_blocks = []
    key_terms = []
    value_terms = []
    for head_at in range(heads_here):
        mixing, out_low = saved[head_at]
        query_tile, key_window, value_window = tiles_of(head_at)
        cols = slice(head_at * HD, (head_at + 1) * HD)
        query_part, key_part, value_part = backward_block(
            query_tile, key_window, value_window, grad_out[:, cols], mixing, out_low
        )
        query_blocks.append(query_part.astype(jnp.bfloat16))
        key_terms.append(cross_rounded(key_part.reshape(3, layer_rows, HD)))
        value_terms.append(cross_rounded(value_part.reshape(3, layer_rows, HD)))
    pair_total = jnp.stack(
        [jnp.concatenate(key_terms, axis=2), jnp.concatenate(value_terms, axis=2)]
    )
    outgoing = jnp.stack([pair_total[:, 0], pair_total[:, 2]]).astype(jnp.bfloat16)
    returned = extended(outgoing, (("ctx", 0),), 1).astype(jnp.float32)
    own_grads = pair_total[:, 1] + returned[0]
    own_grads = own_grads + returned[3]
    key_heads = own_grads[0].astype(jnp.bfloat16)
    value_heads = own_grads[1].astype(jnp.bfloat16)
    query_grad_heads = jnp.concatenate(query_blocks, axis=1)
    return (
        to_tokens(query_grad_heads),
        to_tokens(key_heads),
        to_tokens(value_heads),
        weight_grad,
    )


def solution(mesh):
    in_specs = (
        P("dp", ("ctx", "uly"), None),
        P("dp", ("ctx", "uly"), None),
        P("dp", ("ctx", "uly"), None),
        P("dp", "ctx", None),
        P("uly", None),
        P(),
        P(),
    )
    out_specs = (
        P("dp", ("ctx", "uly"), None),
        P("dp", ("ctx", "uly"), None),
        P("dp", ("ctx", "uly"), None),
        P("uly", None),
    )
    return jax.shard_map(
        on_device, mesh=mesh, in_specs=in_specs, out_specs=out_specs, check_vma=False
    )
```
